256 devices in a mesh: grp: 4 (over y_hi, core), tile: 64 (over y_lo, x, z).
Axes of the slice: x: 4, y: 4 (y_hi: 2, y_lo: 2; y = y_hi * 2 + y_lo), z: 8, core: 2. Of those that a mesh axis runs over, the one named last changes fastest.
Arguments:
- frames: float32 [4, 2048, 2048], P('grp', 'tile'), may hold values from -6 to 6
- otf: float32 [4, 2, 2048, 2048], P('grp', None, 'tile'), may hold values from -6 to 6, as said below
- start_image: float32 [2048, 2048], P('tile'), may hold values from -6 to 6
Outputs:
- consensus: float32 [2048, 2048], P('tile')
The draws below stay inside these ranges and needn't reach their ends.
Inputs may be any that keep to these rules, and one draw needn't show every extreme that they name: Transfer functions of real point spread functions: otf[f, 0, t, s] equals otf[f, 0, -t, -s] and otf[f, 1, t, s] equals -otf[f, 1, -t, -s], indices taken modulo 2048.
All inputs are finite; a program needn't handle non-finite values.
Results may differ from the reference program's by a relative error of at most 0.0001.
Values sent between devices are 32-bit elements; how exact they have to be, the bound alone decides.
No kernel may reach another device: no remote copies, remote signals or barrier semaphores. Data moves between devices by JAX's collectives and lax.ppermute only.
A program may use at most 64 MiB of HBM per device.

```python
import jax
import jax.numpy as jnp
from jax import lax

N = 2048
ITERS = 2
TV_ITERS = 4
FRAMES = 4


def mirror_both(field):
    return jnp.roll(jnp.flip(field, (1, 2)), 1, (1, 2))


def draw_otf(key, part):
    first_key, second_key = jax.random.split(key)
    shape_full = (FRAMES, N, N)
    real_seed = jnp.clip(jax.random.normal(first_key, shape_full, jnp.float32), -4.0, 4.0)
    imag_seed = jnp.clip(jax.random.normal(second_key, shape_full, jnp.float32), -4.0, 4.0)
    real_half = (real_seed + mirror_both(real_seed)) * 0.7071
    imag_half = (imag_seed - mirror_both(imag_seed)) * 0.7071
    return jnp.stack([real_half, imag_half], 1).astype(jnp.float32)


def block_scale(key, dims, pieces, least, top_value):
    loudness, own = 1.0, jax.random.fold_in(key, 6)
    for axis_at, shards_of in pieces:
        heights = jnp.exp(jax.random.uniform(jax.random.fold_in(own, axis_at), (shards_of,), jnp.float32, least / len(pieces), top_value / len(pieces)))
        loudness = loudness * jnp.repeat(heights, dims[axis_at] // shards_of).reshape([-1 if axis == axis_at else 1 for axis in range(len(dims))])
    return loudness


def bell_draw(stream_key, shape, scale, most, shards=(), kind=jnp.bfloat16):
    level = block_scale(stream_key, shape, shards, -0.22, 0.18) if shards else 1.0
    result = jax.random.normal(stream_key, shape, jnp.float32) * scale * level
    return jnp.minimum(jnp.maximum(result, -most), most).astype(kind)


def setup_inputs(seed: int = 0) -> dict:
    splits = jax.random.split(jax.random.key(seed), 4)
    frames = bell_draw(splits[0], (FRAMES, N, N), 1.0, 6.0, ((0, 4), (1, 64)), jnp.float32)
    otf = draw_otf(jax.random.fold_in(splits[3], 71), 0)
    start_image = bell_draw(splits[2], (N, N), 1.0, 6.0, ((0, 64),), jnp.float32)
    return dict(frames=frames, otf=otf, start_image=start_image)


penalty = 1.0
smooth_weight = 0.25
dual_step = 0.125

def gradient(field):
    zero_row = jnp.zeros((1, field.shape[1]), field.dtype)
    zero_col = jnp.zeros((field.shape[0], 1), field.dtype)
    downward = jnp.concatenate([field[1:] - field[:-1], zero_row], 0)
    sideways = jnp.concatenate([field[:, 1:] - field[:, :-1], zero_col], 1)
    return (downward, sideways)

def divergence(downward, sideways):
    zero_row = jnp.zeros((1, downward.shape[1]), downward.dtype)
    zero_col = jnp.zeros((downward.shape[0], 1), downward.dtype)
    prev_rows = jnp.concatenate([zero_row, downward[:-1]], 0)
    prev_cols = jnp.concatenate([zero_col, sideways[:, :-1]], 1)
    return downward - prev_rows + sideways - prev_cols

def denoise(average):
    downward = jnp.zeros_like(average)
    sideways = jnp.zeros_like(average)
    for sweep_index in range(TV_ITERS):
        target = divergence(downward, sideways) - average / smooth_weight
        grad_down, grad_side = gradient(target)
        scaling = 1.0 + dual_step * jnp.sqrt(grad_down * grad_down + grad_side * grad_side)
        downward = (downward + dual_step * grad_down) / scaling
        sideways = (sideways + dual_step * grad_side) / scaling
    return average - smooth_weight * divergence(downward, sideways)

def reference(frames, otf, start_image):
    consensus = start_image
    duals = jnp.zeros_like(frames)
    for iteration in range(ITERS):

        def solve_frame(packed, consensus=consensus):
            image, response, dual_field = packed
            transfer = jnp.transpose(response[0]) + 1j * jnp.transpose(response[1])
            numerator = jnp.conj(transfer) * jnp.fft.fft2(image) + penalty * jnp.fft.fft2(consensus - dual_field)
            denominator = jnp.real(transfer) ** 2 + jnp.imag(transfer) ** 2 + penalty
            return jnp.real(jnp.fft.ifft2(numerator / denominator))
        estimates = lax.map(solve_frame, (frames, otf, duals))
        average = lax.optimization_barrier(jnp.mean(estimates + duals, axis=0))
        consensus = denoise(average)
        duals = duals + estimates - consensus[None]
    return consensus
```

```python
import math

import jax
import jax.numpy as jnp
from jax import lax
from jax.sharding import PartitionSpec as P

ITERS = 2
TV_ITERS = 4


penalty = 1.0
smooth_weight = 0.25
dual_step = 0.125
highest = lax.Precision.HIGHEST


def from_behind(value, axis, steps):
    count = lax.axis_size(axis)
    leading, last = (max(0, -steps), min(count, count - steps))
    return lax.ppermute(value, axis, [(source, source + steps) for source in range(leading, last)])


def angle_table(first_count, second_count, modulus):
    left_index = jnp.arange(first_count, dtype=jnp.int32)[:, None]
    right_index = jnp.arange(second_count, dtype=jnp.int32)[None, :]
    return (left_index * right_index % modulus).astype(jnp.float32) * (2.0 * math.pi / modulus)


def transform_last(real_part, imag_part, sign_value):
    extent = real_part.shape[-1]
    inner_size = 16
    outer_size = extent // inner_size
    leading = real_part.shape[:-1]
    first_angle = angle_table(inner_size, inner_size, inner_size)
    first_cos = jnp.cos(first_angle)
    first_sin = sign_value * jnp.sin(first_angle)
    split_real = real_part.reshape(leading + (inner_size, outer_size))
    mixed_real = jnp.einsum("...an,ak->...kn", split_real, first_cos, precision=highest)
    mixed_imag = jnp.einsum("...an,ak->...kn", split_real, first_sin, precision=highest)
    if imag_part is not None:
        split_imag = imag_part.reshape(leading + (inner_size, outer_size))
        mixed_real = mixed_real - jnp.einsum(
            "...an,ak->...kn", split_imag, first_sin, precision=highest
        )
        mixed_imag = mixed_imag + jnp.einsum(
            "...an,ak->...kn", split_imag, first_cos, precision=highest
        )
    twist_angle = angle_table(inner_size, outer_size, extent)
    twist_cos = jnp.cos(twist_angle)
    twist_sin = sign_value * jnp.sin(twist_angle)
    turned_real = mixed_real * twist_cos - mixed_imag * twist_sin
    turned_imag = mixed_real * twist_sin + mixed_imag * twist_cos
    second_angle = angle_table(outer_size, outer_size, outer_size)
    second_cos = jnp.cos(second_angle)
    second_sin = sign_value * jnp.sin(second_angle)
    out_real = jnp.einsum(
        "...kn,nj->...jk", turned_real, second_cos, precision=highest
    ) - jnp.einsum("...kn,nj->...jk", turned_imag, second_sin, precision=highest)
    out_imag = jnp.einsum(
        "...kn,nj->...jk", turned_real, second_sin, precision=highest
    ) + jnp.einsum("...kn,nj->...jk", turned_imag, second_cos, precision=highest)
    return (out_real.reshape(leading + (extent,)), out_imag.reshape(leading + (extent,)))


def regroup(moved, frame_count, tile_rows, extent):
    tiles = extent // tile_rows
    moved = moved.reshape(tile_rows, tiles, 2, frame_count, tile_rows)
    return jnp.transpose(moved, (2, 3, 0, 1, 4)).reshape(2, frame_count, tile_rows, extent)


def to_spectrum(images):
    frame_count, tile_rows, extent = images.shape
    col_real, col_imag = transform_last(images, None, -1.0)
    packed = jnp.transpose(jnp.stack([col_real, col_imag]), (3, 0, 1, 2)).reshape(
        extent, 2 * frame_count * tile_rows
    )
    moved = lax.all_to_all(packed, "tile", split_axis=0, concat_axis=1, tiled=True)
    moved = regroup(moved, frame_count, tile_rows, extent)
    return transform_last(moved[0], moved[1], -1.0)


def to_image(spec_real, spec_imag):
    frame_count, tile_rows, extent = spec_real.shape
    row_real, row_imag = transform_last(spec_real, spec_imag, 1.0)
    packed = jnp.transpose(jnp.stack([row_real, row_imag]), (3, 0, 1, 2)).reshape(
        extent, 2 * frame_count * tile_rows
    )
    moved = lax.all_to_all(packed, "tile", split_axis=0, concat_axis=1, tiled=True)
    moved = regroup(moved, frame_count, tile_rows, extent)
    image_parts = transform_last(moved[0], moved[1], 1.0)
    return image_parts[0] / float(extent * extent)


def exchange_sum(value, axis):
    count = lax.axis_size(axis)
    step = 1
    while step < count:
        value = value + lax.ppermute(value, axis, [(source, source ^ step) for source in range(count)])
        step *= 2
    return value


def denoise_sweeps(average):
    tile_rows, extent = average.shape
    halo = 8
    total_rows = tile_rows * lax.axis_size("tile")
    above = from_behind(average[-halo:], "tile", 1)
    below = from_behind(average[:halo], "tile", -1)
    padded = jnp.concatenate([above, average, below], 0)
    padded_rows = tile_rows + 2 * halo
    row_index = jnp.arange(padded_rows, dtype=jnp.int32)[:, None]
    global_row = lax.axis_index("tile") * tile_rows - halo + row_index
    col_index = jnp.arange(extent, dtype=jnp.int32)[None, :]
    keep_rows = jnp.where((global_row >= 0) & (global_row < total_rows - 1), 1.0, 0.0).astype(jnp.float32)
    keep_cols = jnp.where(col_index == extent - 1, 0.0, 1.0).astype(jnp.float32)
    zero_col = jnp.zeros((padded_rows, 1), jnp.float32)
    zero_row = jnp.zeros((1, extent), jnp.float32)

    def divergence(downward, sideways):
        prev_rows = jnp.concatenate([zero_row, downward[:-1]], 0)
        prev_cols = jnp.concatenate([zero_col, sideways[:, :-1]], 1)
        return downward - prev_rows + sideways - prev_cols

    downward = jnp.zeros_like(padded)
    sideways = jnp.zeros_like(padded)
    for sweep_index in range(TV_ITERS):
        target = divergence(downward, sideways) - padded / smooth_weight
        next_rows = jnp.concatenate([target[1:], zero_row], 0)
        grad_down = (next_rows - target) * keep_rows
        grad_side = (jnp.concatenate([target[:, 1:], zero_col], 1) - target) * keep_cols
        scaling = 1.0 + dual_step * jnp.sqrt(grad_down * grad_down + grad_side * grad_side)
        downward = (downward + dual_step * grad_down) / scaling
        sideways = (sideways + dual_step * grad_side) / scaling
    result = padded - smooth_weight * divergence(downward, sideways)
    return result[halo : halo + tile_rows]


def denoise(average):
    return denoise_sweeps(average)


def body(frames, otf, start_image):
    frame_count = frames.shape[0]
    total_frames = float(frame_count * lax.axis_size("grp"))
    response_real = otf[:, 0]
    response_imag = otf[:, 1]
    gain = 1.0 / (response_real * response_real + response_imag * response_imag + penalty)
    both_real, both_imag = to_spectrum(jnp.concatenate([frames, start_image[None]], 0))
    data_real, data_imag = both_real[:frame_count], both_imag[:frame_count]
    weighted_real = response_real * data_real + response_imag * data_imag
    weighted_imag = response_real * data_imag - response_imag * data_real
    consensus = start_image
    duals = jnp.zeros_like(frames)
    for iteration in range(ITERS):
        if iteration == 0:
            shifted_real, shifted_imag = both_real[frame_count:], both_imag[frame_count:]
        else:
            shifted_real, shifted_imag = to_spectrum(consensus[None] - duals)
        estimates = to_image(
            (weighted_real + penalty * shifted_real) * gain,
            (weighted_imag + penalty * shifted_imag) * gain,
        )
        partial_sum = jnp.sum(estimates + duals, axis=0)
        average = exchange_sum(partial_sum, "grp") / total_frames
        consensus = denoise(average)
        duals = duals + estimates - consensus[None]
    return consensus


def solution(mesh):
    placed = (P("grp", "tile", None), P("grp", None, "tile", None), P("tile", None))
    return jax.shard_map(
        body, mesh=mesh, in_specs=placed, out_specs=P("tile", None), check_vma=False
    )
```

```python
import math

import jax
import jax.numpy as jnp
from jax import lax
from jax.sharding import PartitionSpec as P

ITERS = 2
TV_ITERS = 4


penalty = 1.0
smooth_weight = 0.25
dual_step = 0.125
highest = lax.Precision.HIGH


def from_behind(value, axis, steps):
    count = lax.axis_size(axis)
    leading, last = (max(0, -steps), min(count, count - steps))
    return lax.ppermute(value, axis, [(source, source + steps) for source in range(leading, last)])


def angle_table(first_count, second_count, modulus):
    left_index = jnp.arange(first_count, dtype=jnp.int32)[:, None]
    right_index = jnp.arange(second_count, dtype=jnp.int32)[None, :]
    return (left_index * right_index % modulus).astype(jnp.float32) * (2.0 * math.pi / modulus)


def transform_last(real_part, imag_part, sign_value):
    extent = real_part.shape[-1]
    inner_size = 16
    outer_size = extent // inner_size
    leading = real_part.shape[:-1]
    first_angle = angle_table(inner_size, inner_size, inner_size)
    first_cos = jnp.cos(first_angle)
    first_sin = sign_value * jnp.sin(first_angle)
    split_real = real_part.reshape(leading + (inner_size, outer_size))
    mixed_real = jnp.einsum("...an,ak->...kn", split_real, first_cos, precision=highest)
    mixed_imag = jnp.einsum("...an,ak->...kn", split_real, first_sin, precision=highest)
    if imag_part is not None:
        split_imag = imag_part.reshape(leading + (inner_size, outer_size))
        mixed_real = mixed_real - jnp.einsum(
            "...an,ak->...kn", split_imag, first_sin, precision=highest
        )
        mixed_imag = mixed_imag + jnp.einsum(
            "...an,ak->...kn", split_imag, first_cos, precision=highest
        )
    twist_angle = angle_table(inner_size, outer_size, extent)
    twist_cos = jnp.cos(twist_angle)
    twist_sin = sign_value * jnp.sin(twist_angle)
    turned_real = mixed_real * twist_cos - mixed_imag * twist_sin
    turned_imag = mixed_real * twist_sin + mixed_imag * twist_cos
    second_angle = angle_table(outer_size, outer_size, outer_size)
    second_cos = jnp.cos(second_angle)
    second_sin = sign_value * jnp.sin(second_angle)
    out_real = jnp.einsum(
        "...kn,nj->...jk", turned_real, second_cos, precision=highest
    ) - jnp.einsum("...kn,nj->...jk", turned_imag, second_sin, precision=highest)
    out_imag = jnp.einsum(
        "...kn,nj->...jk", turned_real, second_sin, precision=highest
    ) + jnp.einsum("...kn,nj->...jk", turned_imag, second_cos, precision=highest)
    return (out_real.reshape(leading + (extent,)), out_imag.reshape(leading + (extent,)))


def regroup(moved, frame_count, tile_rows, extent):
    tiles = extent // tile_rows
    moved = moved.reshape(tile_rows, tiles, 2, frame_count, tile_rows)
    return jnp.transpose(moved, (2, 3, 0, 1, 4)).reshape(2, frame_count, tile_rows, extent)


def to_spectrum(images):
    frame_count, tile_rows, extent = images.shape
    col_real, col_imag = transform_last(images, None, -1.0)
    packed = jnp.transpose(jnp.stack([col_real, col_imag]), (3, 0, 1, 2)).reshape(
        extent, 2 * frame_count * tile_rows
    )
    moved = lax.all_to_all(packed, "tile", split_axis=0, concat_axis=1, tiled=True)
    moved = regroup(moved, frame_count, tile_rows, extent)
    return transform_last(moved[0], moved[1], -1.0)


def to_image(spec_real, spec_imag):
    frame_count, tile_rows, extent = spec_real.shape
    row_real, row_imag = transform_last(spec_real, spec_imag, 1.0)
    packed = jnp.transpose(jnp.stack([row_real, row_imag]), (3, 0, 1, 2)).reshape(
        extent, 2 * frame_count * tile_rows
    )
    moved = lax.all_to_all(packed, "tile", split_axis=0, concat_axis=1, tiled=True)
    moved = regroup(moved, frame_count, tile_rows, extent)
    image_parts = transform_last(moved[0], moved[1], 1.0)
    return image_parts[0] / float(extent * extent)


def exchange_sum(value, axis):
    count = lax.axis_size(axis)
    step = 1
    while step < count:
        value = value + lax.ppermute(value, axis, [(source, source ^ step) for source in range(count)])
        step *= 2
    return value


def denoise_sweeps(average):
    tile_rows, extent = average.shape
    halo = 8
    total_rows = tile_rows * lax.axis_size("tile")
    above = from_behind(average[-halo:], "tile", 1)
    below = from_behind(average[:halo], "tile", -1)
    padded = jnp.concatenate([above, average, below], 0)
    padded_rows = tile_rows + 2 * halo
    row_index = jnp.arange(padded_rows, dtype=jnp.int32)[:, None]
    global_row = lax.axis_index("tile") * tile_rows - halo + row_index
    col_index = jnp.arange(extent, dtype=jnp.int32)[None, :]
    keep_rows = jnp.where((global_row >= 0) & (global_row < total_rows - 1), 1.0, 0.0).astype(jnp.float32)
    keep_cols = jnp.where(col_index == extent - 1, 0.0, 1.0).astype(jnp.float32)
    zero_col = jnp.zeros((padded_rows, 1), jnp.float32)
    zero_row = jnp.zeros((1, extent), jnp.float32)

    def divergence(downward, sideways):
        prev_rows = jnp.concatenate([zero_row, downward[:-1]], 0)
        prev_cols = jnp.concatenate([zero_col, sideways[:, :-1]], 1)
        return downward - prev_rows + sideways - prev_cols

    downward = jnp.zeros_like(padded)
    sideways = jnp.zeros_like(padded)
    for sweep_index in range(TV_ITERS):
        target = divergence(downward, sideways) - padded / smooth_weight
        next_rows = jnp.concatenate([target[1:], zero_row], 0)
        grad_down = (next_rows - target) * keep_rows
        grad_side = (jnp.concatenate([target[:, 1:], zero_col], 1) - target) * keep_cols
        scaling = 1.0 + dual_step * jnp.sqrt(grad_down * grad_down + grad_side * grad_side)
        downward = (downward + dual_step * grad_down) / scaling
        sideways = (sideways + dual_step * grad_side) / scaling
    result = padded - smooth_weight * divergence(downward, sideways)
    return result[halo : halo + tile_rows]


def denoise(average):
    return denoise_sweeps(average)


def body(frames, otf, start_image):
    frame_count = frames.shape[0]
    total_frames = float(frame_count * lax.axis_size("grp"))
    response_real = otf[:, 0]
    response_imag = otf[:, 1]
    gain = 1.0 / (response_real * response_real + response_imag * response_imag + penalty)
    both_real, both_imag = to_spectrum(jnp.concatenate([frames, start_image[None]], 0))
    data_real, data_imag = both_real[:frame_count], both_imag[:frame_count]
    weighted_real = response_real * data_real + response_imag * data_imag
    weighted_imag = response_real * data_imag - response_imag * data_real
    consensus = start_image
    duals = jnp.zeros_like(frames)
    for iteration in range(ITERS):
        if iteration == 0:
            shifted_real, shifted_imag = both_real[frame_count:], both_imag[frame_count:]
        else:
            shifted_real, shifted_imag = to_spectrum(consensus[None] - duals)
        estimates = to_image(
            (weighted_real + penalty * shifted_real) * gain,
            (weighted_imag + penalty * shifted_imag) * gain,
        )
        partial_sum = jnp.sum(estimates + duals, axis=0)
        average = exchange_sum(partial_sum, "grp") / total_frames
        consensus = denoise(average)
        duals = duals + estimates - consensus[None]
    return consensus


def solution(mesh):
    placed = (P("grp", "tile", None), P("grp", None, "tile", None), P("tile", None))
    return jax.shard_map(
        body, mesh=mesh, in_specs=placed, out_specs=P("tile", None), check_vma=False
    )
```

```python
import math

import jax
import jax.numpy as jnp
from jax import lax
from jax.sharding import PartitionSpec as P

ITERS = 2
TV_ITERS = 4


penalty = 1.0
smooth_weight = 0.25
dual_step = 0.125
highest = lax.Precision.HIGHEST


def from_behind(value, axis, steps):
    count = lax.axis_size(axis)
    leading, last = (max(0, -steps), min(count, count - steps))
    return lax.ppermute(value, axis, [(source, source + steps) for source in range(leading, last)])


def angle_table(first_count, second_count, modulus):
    left_index = jnp.arange(first_count, dtype=jnp.int32)[:, None]
    right_index = jnp.arange(second_count, dtype=jnp.int32)[None, :]
    return (left_index * right_index % modulus).astype(jnp.float32) * (2.0 * math.pi / modulus)


def transform_last(real_part, imag_part, sign_value):
    extent = real_part.shape[-1]
    inner_size = 16
    outer_size = extent // inner_size
    leading = real_part.shape[:-1]
    first_angle = angle_table(inner_size, inner_size, inner_size)
    first_cos = jnp.cos(first_angle)
    first_sin = sign_value * jnp.sin(first_angle)
    split_real = real_part.reshape(leading + (inner_size, outer_size))
    mixed_real = jnp.einsum("...an,ak->...kn", split_real, first_cos, precision=highest)
    mixed_imag = jnp.einsum("...an,ak->...kn", split_real, first_sin, precision=highest)
    if imag_part is not None:
        split_imag = imag_part.reshape(leading + (inner_size, outer_size))
        mixed_real = mixed_real - jnp.einsum(
            "...an,ak->...kn", split_imag, first_sin, precision=highest
        )
        mixed_imag = mixed_imag + jnp.einsum(
            "...an,ak->...kn", split_imag, first_cos, precision=highest
        )
    twist_angle = angle_table(inner_size, outer_size, extent)
    twist_cos = jnp.cos(twist_angle)
    twist_sin = sign_value * jnp.sin(twist_angle)
    turned_real = mixed_real * twist_cos - mixed_imag * twist_sin
    turned_imag = mixed_real * twist_sin + mixed_imag * twist_cos
    second_angle = angle_table(outer_size, outer_size, outer_size)
    second_cos = jnp.cos(second_angle)
    second_sin = sign_value * jnp.sin(second_angle)
    out_real = jnp.einsum(
        "...kn,nj->...jk", turned_real, second_cos, precision=highest
    ) - jnp.einsum("...kn,nj->...jk", turned_imag, second_sin, precision=highest)
    out_imag = jnp.einsum(
        "...kn,nj->...jk", turned_real, second_sin, precision=highest
    ) + jnp.einsum("...kn,nj->...jk", turned_imag, second_cos, precision=highest)
    return (out_real.reshape(leading + (extent,)), out_imag.reshape(leading + (extent,)))


def regroup(moved, frame_count, tile_rows, extent):
    tiles = extent // tile_rows
    moved = moved.reshape(tile_rows, tiles, 2, frame_count, tile_rows)
    return jnp.transpose(moved, (2, 3, 0, 1, 4)).reshape(2, frame_count, tile_rows, extent)


def to_spectrum(images):
    frame_count, tile_rows, extent = images.shape
    col_real, col_imag = transform_last(images, None, -1.0)
    packed = jnp.transpose(jnp.stack([col_real, col_imag]), (3, 0, 1, 2)).reshape(
        extent, 2 * frame_count * tile_rows
    )
    moved = lax.all_to_all(packed, "tile", split_axis=0, concat_axis=1, tiled=True)
    moved = regroup(moved, frame_count, tile_rows, extent)
    return transform_last(moved[0], moved[1], -1.0)


def to_image(spec_real, spec_imag):
    frame_count, tile_rows, extent = spec_real.shape
    row_real, row_imag = transform_last(spec_real, spec_imag, 1.0)
    packed = jnp.transpose(jnp.stack([row_real, row_imag]), (3, 0, 1, 2)).reshape(
        extent, 2 * frame_count * tile_rows
    )
    moved = lax.all_to_all(packed, "tile", split_axis=0, concat_axis=1, tiled=True)
    moved = regroup(moved, frame_count, tile_rows, extent)
    image_parts = transform_last(moved[0], moved[1], 1.0)
    return image_parts[0] / float(extent * extent)


ALL_AXES = ("grp", "tile")


def flat_index():
    return lax.axis_index("tile") * lax.axis_size("grp") + lax.axis_index("grp")


def flat_count():
    return lax.axis_size("tile") * lax.axis_size("grp")


def flat_shift(value, steps):
    tiles, groups = lax.axis_size("tile"), lax.axis_size("grp")
    count = tiles * groups
    leading, last = (max(0, -steps), min(count, count - steps))

    def place(owner):
        return (owner % groups) * tiles + owner // groups

    pairs = [(place(source), place(source + steps)) for source in range(leading, last)]
    return lax.ppermute(value, ALL_AXES, pairs)


def inverse_to_rows(spec_real, spec_imag):
    frame_count, block, extent = spec_real.shape
    tiles, groups = lax.axis_size("tile"), lax.axis_size("grp")
    owners = tiles * groups
    own_rows = extent // owners
    row_real, row_imag = transform_last(spec_real, spec_imag, 1.0)
    packed = jnp.stack([row_real, row_imag]).reshape(2, frame_count, block, tiles, groups, own_rows)
    packed = jnp.transpose(packed, (4, 3, 0, 1, 2, 5)).reshape(owners, 2, frame_count, block, own_rows)
    moved = lax.all_to_all(packed, ALL_AXES, 0, 0, tiled=True)
    moved = moved.reshape(groups, tiles, 2, frame_count, block, own_rows)
    summed = jnp.sum(moved, axis=(0, 3))
    summed = jnp.transpose(summed, (1, 3, 0, 2)).reshape(2, own_rows, tiles * block)
    image_parts = transform_last(summed[0], summed[1], 1.0)
    return image_parts[0] / float(extent * extent)


def forward_from_rows(rows):
    own_rows, extent = rows.shape
    tiles, groups = lax.axis_size("tile"), lax.axis_size("grp")
    block = extent // tiles
    col_real, col_imag = transform_last(rows, None, -1.0)
    packed = jnp.stack([col_real, col_imag]).reshape(2, own_rows, tiles, block)
    packed = jnp.transpose(packed, (2, 0, 3, 1))[None]
    packed = jnp.broadcast_to(packed, (groups, tiles, 2, block, own_rows))
    packed = packed.reshape(groups * tiles, 2, block, own_rows)
    moved = lax.all_to_all(packed, ALL_AXES, 0, 0, tiled=True)
    moved = moved.reshape(groups, tiles, 2, block, own_rows)
    moved = jnp.transpose(moved, (2, 3, 1, 0, 4)).reshape(2, block, extent)
    spec_real, spec_imag = transform_last(moved[0], moved[1], -1.0)
    return spec_real[None], spec_imag[None]


def denoise_rows(average):
    own_rows, extent = average.shape
    halo = 8
    total_rows = own_rows * flat_count()
    above = flat_shift(average[-halo:], 1)
    below = flat_shift(average[:halo], -1)
    padded = jnp.concatenate([above, average, below], 0)
    padded_rows = own_rows + 2 * halo
    row_index = jnp.arange(padded_rows, dtype=jnp.int32)[:, None]
    global_row = flat_index() * own_rows - halo + row_index
    col_index = jnp.arange(extent, dtype=jnp.int32)[None, :]
    keep_rows = jnp.where((global_row >= 0) & (global_row < total_rows - 1), 1.0, 0.0).astype(jnp.float32)
    keep_cols = jnp.where(col_index == extent - 1, 0.0, 1.0).astype(jnp.float32)
    zero_col = jnp.zeros((padded_rows, 1), jnp.float32)
    zero_row = jnp.zeros((1, extent), jnp.float32)

    def divergence(downward, sideways):
        prev_rows = jnp.concatenate([zero_row, downward[:-1]], 0)
        prev_cols = jnp.concatenate([zero_col, sideways[:, :-1]], 1)
        return downward - prev_rows + sideways - prev_cols

    downward = jnp.zeros_like(padded)
    sideways = jnp.zeros_like(padded)
    for sweep_index in range(TV_ITERS):
        target = divergence(downward, sideways) - padded / smooth_weight
        next_rows = jnp.concatenate([target[1:], zero_row], 0)
        grad_down = (next_rows - target) * keep_rows
        grad_side = (jnp.concatenate([target[:, 1:], zero_col], 1) - target) * keep_cols
        scaling = 1.0 + dual_step * jnp.sqrt(grad_down * grad_down + grad_side * grad_side)
        downward = (downward + dual_step * grad_down) / scaling
        sideways = (sideways + dual_step * grad_side) / scaling
    result = padded - smooth_weight * divergence(downward, sideways)
    return result[halo : halo + own_rows]


def body(frames, otf, start_image):
    frame_count = frames.shape[0]
    total_frames = float(frame_count * lax.axis_size("grp"))
    response_real = otf[:, 0]
    response_imag = otf[:, 1]
    gain = 1.0 / (response_real * response_real + response_imag * response_imag + penalty)
    both_real, both_imag = to_spectrum(jnp.concatenate([frames, start_image[None]], 0))
    data_real, data_imag = both_real[:frame_count], both_imag[:frame_count]
    weighted_real = response_real * data_real + response_imag * data_imag
    weighted_imag = response_real * data_imag - response_imag * data_real
    center_real, center_imag = both_real[frame_count:], both_imag[frame_count:]
    dual_real = jnp.zeros_like(data_real)
    dual_imag = jnp.zeros_like(data_imag)
    for iteration in range(ITERS):
        estimate_real = (weighted_real + penalty * (center_real - dual_real)) * gain
        estimate_imag = (weighted_imag + penalty * (center_imag - dual_imag)) * gain
        average = inverse_to_rows(estimate_real + dual_real, estimate_imag + dual_imag) / total_frames
        consensus_rows = denoise_rows(average)
        if iteration + 1 < ITERS:
            center_real, center_imag = forward_from_rows(consensus_rows)
            dual_real = dual_real + estimate_real - center_real
            dual_imag = dual_imag + estimate_imag - center_imag
    return lax.all_gather(consensus_rows, "grp", axis=0, tiled=True)


def solution(mesh):
    placed = (P("grp", "tile", None), P("grp", None, "tile", None), P("tile", None))
    return jax.shard_map(
        body, mesh=mesh, in_specs=placed, out_specs=P("tile", None), check_vma=False
    )
```

```python
import math

import jax
import jax.numpy as jnp
from jax import lax
from jax.sharding import PartitionSpec as P

ITERS = 2
TV_ITERS = 4


penalty = 1.0
smooth_weight = 0.25
dual_step = 0.125
highest = lax.Precision.HIGHEST


def from_behind(value, axis, steps):
    count = lax.axis_size(axis)
    leading, last = (max(0, -steps), min(count, count - steps))
    return lax.ppermute(value, axis, [(source, source + steps) for source in range(leading, last)])


def angle_table(first_count, second_count, modulus):
    left_index = jnp.arange(first_count, dtype=jnp.int32)[:, None]
    right_index = jnp.arange(second_count, dtype=jnp.int32)[None, :]
    return (left_index * right_index % modulus).astype(jnp.float32) * (2.0 * math.pi / modulus)


def transform_last(real_part, imag_part, sign_value):
    extent = real_part.shape[-1]
    inner_size = 16
    outer_size = extent // inner_size
    leading = real_part.shape[:-1]
    first_angle = angle_table(inner_size, inner_size, inner_size)
    first_cos = jnp.cos(first_angle)
    first_sin = sign_value * jnp.sin(first_angle)
    split_real = real_part.reshape(leading + (inner_size, outer_size))
    mixed_real = jnp.einsum("...an,ak->...kn", split_real, first_cos, precision=highest)
    mixed_imag = jnp.einsum("...an,ak->...kn", split_real, first_sin, precision=highest)
    if imag_part is not None:
        split_imag = imag_part.reshape(leading + (inner_size, outer_size))
        mixed_real = mixed_real - jnp.einsum(
            "...an,ak->...kn", split_imag, first_sin, precision=highest
        )
        mixed_imag = mixed_imag + jnp.einsum(
            "...an,ak->...kn", split_imag, first_cos, precision=highest
        )
    twist_angle = angle_table(inner_size, outer_size, extent)
    twist_cos = jnp.cos(twist_angle)
    twist_sin = sign_value * jnp.sin(twist_angle)
    turned_real = mixed_real * twist_cos - mixed_imag * twist_sin
    turned_imag = mixed_real * twist_sin + mixed_imag * twist_cos
    second_angle = angle_table(outer_size, outer_size, outer_size)
    second_cos = jnp.cos(second_angle)
    second_sin = sign_value * jnp.sin(second_angle)
    out_real = jnp.einsum(
        "...kn,nj->...jk", turned_real, second_cos, precision=highest
    ) - jnp.einsum("...kn,nj->...jk", turned_imag, second_sin, precision=highest)
    out_imag = jnp.einsum(
        "...kn,nj->...jk", turned_real, second_sin, precision=highest
    ) + jnp.einsum("...kn,nj->...jk", turned_imag, second_cos, precision=highest)
    return (out_real.reshape(leading + (extent,)), out_imag.reshape(leading + (extent,)))


def transform_scrambled(real_part, imag_part, sign_value):
    extent = real_part.shape[-1]
    inner_size = 16
    outer_size = extent // inner_size
    leading = real_part.shape[:-1]
    first_angle = angle_table(inner_size, inner_size, inner_size)
    first_cos = jnp.cos(first_angle)
    first_sin = sign_value * jnp.sin(first_angle)
    split_real = real_part.reshape(leading + (inner_size, outer_size))
    split_imag = imag_part.reshape(leading + (inner_size, outer_size))
    mixed_real = jnp.einsum("...an,ak->...kn", split_real, first_cos, precision=highest) - jnp.einsum(
        "...an,ak->...kn", split_imag, first_sin, precision=highest
    )
    mixed_imag = jnp.einsum("...an,ak->...kn", split_real, first_sin, precision=highest) + jnp.einsum(
        "...an,ak->...kn", split_imag, first_cos, precision=highest
    )
    twist_angle = angle_table(inner_size, outer_size, extent)
    twist_cos = jnp.cos(twist_angle)
    twist_sin = sign_value * jnp.sin(twist_angle)
    turned_real = mixed_real * twist_cos - mixed_imag * twist_sin
    turned_imag = mixed_real * twist_sin + mixed_imag * twist_cos
    second_angle = angle_table(outer_size, outer_size, outer_size)
    second_cos = jnp.cos(second_angle)
    second_sin = sign_value * jnp.sin(second_angle)
    out_real = jnp.einsum(
        "...kn,nj->...kj", turned_real, second_cos, precision=highest
    ) - jnp.einsum("...kn,nj->...kj", turned_imag, second_sin, precision=highest)
    out_imag = jnp.einsum(
        "...kn,nj->...kj", turned_real, second_sin, precision=highest
    ) + jnp.einsum("...kn,nj->...kj", turned_imag, second_cos, precision=highest)
    return (out_real.reshape(leading + (extent,)), out_imag.reshape(leading + (extent,)))


def transform_unscramble(real_part, imag_part, sign_value):
    extent = real_part.shape[-1]
    inner_size = 16
    outer_size = extent // inner_size
    leading = real_part.shape[:-1]
    split_real = real_part.reshape(leading + (inner_size, outer_size))
    split_imag = imag_part.reshape(leading + (inner_size, outer_size))
    second_angle = angle_table(outer_size, outer_size, outer_size)
    second_cos = jnp.cos(second_angle)
    second_sin = sign_value * jnp.sin(second_angle)
    mixed_real = jnp.einsum("...kj,jn->...kn", split_real, second_cos, precision=highest) - jnp.einsum(
        "...kj,jn->...kn", split_imag, second_sin, precision=highest
    )
    mixed_imag = jnp.einsum("...kj,jn->...kn", split_real, second_sin, precision=highest) + jnp.einsum(
        "...kj,jn->...kn", split_imag, second_cos, precision=highest
    )
    twist_angle = angle_table(inner_size, outer_size, extent)
    twist_cos = jnp.cos(twist_angle)
    twist_sin = sign_value * jnp.sin(twist_angle)
    turned_real = mixed_real * twist_cos - mixed_imag * twist_sin
    turned_imag = mixed_real * twist_sin + mixed_imag * twist_cos
    first_angle = angle_table(inner_size, inner_size, inner_size)
    first_cos = jnp.cos(first_angle)
    first_sin = sign_value * jnp.sin(first_angle)
    out_real = jnp.einsum(
        "...kn,ka->...an", turned_real, first_cos, precision=highest
    ) - jnp.einsum("...kn,ka->...an", turned_imag, first_sin, precision=highest)
    out_imag = jnp.einsum(
        "...kn,ka->...an", turned_real, first_sin, precision=highest
    ) + jnp.einsum("...kn,ka->...an", turned_imag, first_cos, precision=highest)
    return (out_real.reshape(leading + (extent,)), out_imag.reshape(leading + (extent,)))


def scramble_last(values):
    extent = values.shape[-1]
    inner_size = 16
    split = values.reshape(values.shape[:-1] + (extent // inner_size, inner_size))
    return jnp.swapaxes(split, -1, -2).reshape(values.shape)


def gather_groups(rows):
    groups = lax.axis_size("grp")
    position = lax.axis_index("grp")
    step = 1
    while step < groups:
        other = lax.ppermute(rows, "grp", [(source, source ^ step) for source in range(groups)])
        upper = (position // step) % 2 == 1
        rows = jnp.where(upper, jnp.concatenate([other, rows], 0), jnp.concatenate([rows, other], 0))
        step *= 2
    return rows


def regroup(moved, frame_count, tile_rows, extent):
    tiles = extent // tile_rows
    moved = moved.reshape(tile_rows, tiles, 2, frame_count, tile_rows)
    return jnp.transpose(moved, (2, 3, 0, 1, 4)).reshape(2, frame_count, tile_rows, extent)


def to_spectrum(images):
    frame_count, tile_rows, extent = images.shape
    col_real, col_imag = transform_last(images, None, -1.0)
    packed = jnp.transpose(jnp.stack([col_real, col_imag]), (3, 0, 1, 2)).reshape(
        extent, 2 * frame_count * tile_rows
    )
    moved = lax.all_to_all(packed, "tile", split_axis=0, concat_axis=1, tiled=True)
    moved = regroup(moved, frame_count, tile_rows, extent)
    return transform_scrambled(moved[0], moved[1], -1.0)


def to_image(spec_real, spec_imag):
    frame_count, tile_rows, extent = spec_real.shape
    row_real, row_imag = transform_last(spec_real, spec_imag, 1.0)
    packed = jnp.transpose(jnp.stack([row_real, row_imag]), (3, 0, 1, 2)).reshape(
        extent, 2 * frame_count * tile_rows
    )
    moved = lax.all_to_all(packed, "tile", split_axis=0, concat_axis=1, tiled=True)
    moved = regroup(moved, frame_count, tile_rows, extent)
    image_parts = transform_last(moved[0], moved[1], 1.0)
    return image_parts[0] / float(extent * extent)


ALL_AXES = ("grp", "tile")


def flat_index():
    return lax.axis_index("tile") * lax.axis_size("grp") + lax.axis_index("grp")


def flat_count():
    return lax.axis_size("tile") * lax.axis_size("grp")


def flat_shift(value, steps):
    tiles, groups = lax.axis_size("tile"), lax.axis_size("grp")
    count = tiles * groups
    leading, last = (max(0, -steps), min(count, count - steps))

    def place(owner):
        return (owner % groups) * tiles + owner // groups

    pairs = [(place(source), place(source + steps)) for source in range(leading, last)]
    return lax.ppermute(value, ALL_AXES, pairs)


def inverse_to_rows(spec_real, spec_imag):
    frame_count, block, extent = spec_real.shape
    tiles, groups = lax.axis_size("tile"), lax.axis_size("grp")
    owners = tiles * groups
    own_rows = extent // owners
    row_real, row_imag = transform_unscramble(spec_real, spec_imag, 1.0)
    packed = jnp.stack([row_real, row_imag]).reshape(2, frame_count, block, tiles, groups, own_rows)
    packed = jnp.transpose(packed, (4, 3, 0, 1, 2, 5)).reshape(owners, 2, frame_count, block, own_rows)
    moved = lax.all_to_all(packed, ALL_AXES, 0, 0, tiled=True)
    moved = moved.reshape(groups, tiles, 2, frame_count, block, own_rows)
    summed = jnp.sum(moved, axis=(0, 3))
    summed = jnp.transpose(summed, (1, 3, 0, 2)).reshape(2, own_rows, tiles * block)
    image_parts = transform_last(summed[0], summed[1], 1.0)
    return image_parts[0] / float(extent * extent)


def forward_from_rows(rows):
    own_rows, extent = rows.shape
    tiles, groups = lax.axis_size("tile"), lax.axis_size("grp")
    block = extent // tiles
    col_real, col_imag = transform_last(rows, None, -1.0)
    packed = jnp.stack([col_real, col_imag]).reshape(2, own_rows, tiles, block)
    packed = jnp.transpose(packed, (2, 0, 3, 1))[None]
    packed = jnp.broadcast_to(packed, (groups, tiles, 2, block, own_rows))
    packed = packed.reshape(groups * tiles, 2, block, own_rows)
    moved = lax.all_to_all(packed, ALL_AXES, 0, 0, tiled=True)
    moved = moved.reshape(groups, tiles, 2, block, own_rows)
    moved = jnp.transpose(moved, (2, 3, 1, 0, 4)).reshape(2, block, extent)
    spec_real, spec_imag = transform_scrambled(moved[0], moved[1], -1.0)
    return spec_real[None], spec_imag[None]


def denoise_rows(average):
    own_rows, extent = average.shape
    halo = 8
    total_rows = own_rows * flat_count()
    above = flat_shift(average[-halo:], 1)
    below = flat_shift(average[:halo], -1)
    padded = jnp.concatenate([above, average, below], 0)
    padded_rows = own_rows + 2 * halo
    row_index = jnp.arange(padded_rows, dtype=jnp.int32)[:, None]
    global_row = flat_index() * own_rows - halo + row_index
    col_index = jnp.arange(extent, dtype=jnp.int32)[None, :]
    keep_rows = jnp.where((global_row >= 0) & (global_row < total_rows - 1), 1.0, 0.0).astype(jnp.float32)
    keep_cols = jnp.where(col_index == extent - 1, 0.0, 1.0).astype(jnp.float32)
    zero_col = jnp.zeros((padded_rows, 1), jnp.float32)
    zero_row = jnp.zeros((1, extent), jnp.float32)

    def divergence(downward, sideways):
        prev_rows = jnp.concatenate([zero_row, downward[:-1]], 0)
        prev_cols = jnp.concatenate([zero_col, sideways[:, :-1]], 1)
        return downward - prev_rows + sideways - prev_cols

    downward = jnp.zeros_like(padded)
    sideways = jnp.zeros_like(padded)
    for sweep_index in range(TV_ITERS):
        target = divergence(downward, sideways) - padded / smooth_weight
        next_rows = jnp.concatenate([target[1:], zero_row], 0)
        grad_down = (next_rows - target) * keep_rows
        grad_side = (jnp.concatenate([target[:, 1:], zero_col], 1) - target) * keep_cols
        scaling = 1.0 + dual_step * jnp.sqrt(grad_down * grad_down + grad_side * grad_side)
        downward = (downward + dual_step * grad_down) / scaling
        sideways = (sideways + dual_step * grad_side) / scaling
    result = padded - smooth_weight * divergence(downward, sideways)
    return result[halo : halo + own_rows]


def body(frames, otf, start_image):
    frame_count = frames.shape[0]
    total_frames = float(frame_count * lax.axis_size("grp"))
    response_real = scramble_last(otf[:, 0])
    response_imag = scramble_last(otf[:, 1])
    gain = 1.0 / (response_real * response_real + response_imag * response_imag + penalty)
    both_real, both_imag = to_spectrum(jnp.concatenate([frames, start_image[None]], 0))
    data_real, data_imag = both_real[:frame_count], both_imag[:frame_count]
    weighted_real = response_real * data_real + response_imag * data_imag
    weighted_imag = response_real * data_imag - response_imag * data_real
    center_real, center_imag = both_real[frame_count:], both_imag[frame_count:]
    dual_real = jnp.zeros_like(data_real)
    dual_imag = jnp.zeros_like(data_imag)
    for iteration in range(ITERS):
        estimate_real = (weighted_real + penalty * (center_real - dual_real)) * gain
        estimate_imag = (weighted_imag + penalty * (center_imag - dual_imag)) * gain
        average = inverse_to_rows(estimate_real + dual_real, estimate_imag + dual_imag) / total_frames
        consensus_rows = denoise_rows(average)
        if iteration + 1 < ITERS:
            center_real, center_imag = forward_from_rows(consensus_rows)
            dual_real = dual_real + estimate_real - center_real
            dual_imag = dual_imag + estimate_imag - center_imag
    return gather_groups(consensus_rows)


def solution(mesh):
    placed = (P("grp", "tile", None), P("grp", None, "tile", None), P("tile", None))
    return jax.shard_map(
        body, mesh=mesh, in_specs=placed, out_specs=P("tile", None), check_vma=False
    )
```

```python
import math

import jax
import jax.numpy as jnp
from jax import lax
from jax.sharding import PartitionSpec as P

ITERS = 2
TV_ITERS = 4


penalty = 1.0
smooth_weight = 0.25
dual_step = 0.125
highest = lax.Precision.HIGHEST


def from_behind(value, axis, steps):
    count = lax.axis_size(axis)
    leading, last = (max(0, -steps), min(count, count - steps))
    return lax.ppermute(value, axis, [(source, source + steps) for source in range(leading, last)])


def angle_table(first_count, second_count, modulus):
    left_index = jnp.arange(first_count, dtype=jnp.int32)[:, None]
    right_index = jnp.arange(second_count, dtype=jnp.int32)[None, :]
    return (left_index * right_index % modulus).astype(jnp.float32) * (2.0 * math.pi / modulus)


def mix(spec, real_part, imag_part, table_cos, table_sin, axis):
    size = table_cos.shape[1]
    table = jnp.concatenate([table_cos, table_sin], axis=1)
    if imag_part is None:
        both = jnp.einsum(spec, real_part, table, precision=highest)
        return lax.slice_in_dim(both, 0, size, axis=axis), lax.slice_in_dim(both, size, 2 * size, axis=axis)
    both = jnp.einsum(spec, jnp.stack([real_part, imag_part]), table, precision=highest)
    with_cos = lax.slice_in_dim(both, 0, size, axis=axis)
    with_sin = lax.slice_in_dim(both, size, 2 * size, axis=axis)
    return with_cos[0] - with_sin[1], with_sin[0] + with_cos[1]


def transform_last(real_part, imag_part, sign_value):
    extent = real_part.shape[-1]
    inner_size = 16
    outer_size = extent // inner_size
    leading = real_part.shape[:-1]
    first_angle = angle_table(inner_size, inner_size, inner_size)
    first_cos = jnp.cos(first_angle)
    first_sin = sign_value * jnp.sin(first_angle)
    split_real = real_part.reshape(leading + (inner_size, outer_size))
    split_imag = None if imag_part is None else imag_part.reshape(leading + (inner_size, outer_size))
    mixed_real, mixed_imag = mix("...an,ak->...kn", split_real, split_imag, first_cos, first_sin, -2)
    twist_angle = angle_table(inner_size, outer_size, extent)
    twist_cos = jnp.cos(twist_angle)
    twist_sin = sign_value * jnp.sin(twist_angle)
    turned_real = mixed_real * twist_cos - mixed_imag * twist_sin
    turned_imag = mixed_real * twist_sin + mixed_imag * twist_cos
    second_angle = angle_table(outer_size, outer_size, outer_size)
    second_cos = jnp.cos(second_angle)
    second_sin = sign_value * jnp.sin(second_angle)
    out_real, out_imag = mix("...kn,nj->...jk", turned_real, turned_imag, second_cos, second_sin, -2)
    return (out_real.reshape(leading + (extent,)), out_imag.reshape(leading + (extent,)))


def transform_scrambled(real_part, imag_part, sign_value):
    extent = real_part.shape[-1]
    inner_size = 16
    outer_size = extent // inner_size
    leading = real_part.shape[:-1]
    first_angle = angle_table(inner_size, inner_size, inner_size)
    first_cos = jnp.cos(first_angle)
    first_sin = sign_value * jnp.sin(first_angle)
    split_real = real_part.reshape(leading + (inner_size, outer_size))
    split_imag = imag_part.reshape(leading + (inner_size, outer_size))
    mixed_real, mixed_imag = mix("...an,ak->...kn", split_real, split_imag, first_cos, first_sin, -2)
    twist_angle = angle_table(inner_size, outer_size, extent)
    twist_cos = jnp.cos(twist_angle)
    twist_sin = sign_value * jnp.sin(twist_angle)
    turned_real = mixed_real * twist_cos - mixed_imag * twist_sin
    turned_imag = mixed_real * twist_sin + mixed_imag * twist_cos
    second_angle = angle_table(outer_size, outer_size, outer_size)
    second_cos = jnp.cos(second_angle)
    second_sin = sign_value * jnp.sin(second_angle)
    out_real, out_imag = mix("...kn,nj->...kj", turned_real, turned_imag, second_cos, second_sin, -1)
    return (out_real.reshape(leading + (extent,)), out_imag.reshape(leading + (extent,)))


def transform_unscramble(real_part, imag_part, sign_value):
    extent = real_part.shape[-1]
    inner_size = 16
    outer_size = extent // inner_size
    leading = real_part.shape[:-1]
    split_real = real_part.reshape(leading + (inner_size, outer_size))
    split_imag = imag_part.reshape(leading + (inner_size, outer_size))
    second_angle = angle_table(outer_size, outer_size, outer_size)
    second_cos = jnp.cos(second_angle)
    second_sin = sign_value * jnp.sin(second_angle)
    mixed_real, mixed_imag = mix("...kj,jn->...kn", split_real, split_imag, second_cos, second_sin, -1)
    twist_angle = angle_table(inner_size, outer_size, extent)
    twist_cos = jnp.cos(twist_angle)
    twist_sin = sign_value * jnp.sin(twist_angle)
    turned_real = mixed_real * twist_cos - mixed_imag * twist_sin
    turned_imag = mixed_real * twist_sin + mixed_imag * twist_cos
    first_angle = angle_table(inner_size, inner_size, inner_size)
    first_cos = jnp.cos(first_angle)
    first_sin = sign_value * jnp.sin(first_angle)
    out_real, out_imag = mix("...kn,ka->...an", turned_real, turned_imag, first_cos, first_sin, -2)
    return (out_real.reshape(leading + (extent,)), out_imag.reshape(leading + (extent,)))


def scramble_last(values):
    extent = values.shape[-1]
    inner_size = 16
    split = values.reshape(values.shape[:-1] + (extent // inner_size, inner_size))
    return jnp.swapaxes(split, -1, -2).reshape(values.shape)


def gather_groups(rows):
    groups = lax.axis_size("grp")
    position = lax.axis_index("grp")
    step = 1
    while step < groups:
        other = lax.ppermute(rows, "grp", [(source, source ^ step) for source in range(groups)])
        upper = (position // step) % 2 == 1
        rows = jnp.where(upper, jnp.concatenate([other, rows], 0), jnp.concatenate([rows, other], 0))
        step *= 2
    return rows


def regroup(moved, frame_count, tile_rows, extent):
    tiles = extent // tile_rows
    moved = moved.reshape(tile_rows, tiles, 2, frame_count, tile_rows)
    return jnp.transpose(moved, (2, 3, 0, 1, 4)).reshape(2, frame_count, tile_rows, extent)


def to_spectrum(images):
    frame_count, tile_rows, extent = images.shape
    col_real, col_imag = transform_last(images, None, -1.0)
    packed = jnp.transpose(jnp.stack([col_real, col_imag]), (3, 0, 1, 2)).reshape(
        extent, 2 * frame_count * tile_rows
    )
    moved = lax.all_to_all(packed, "tile", split_axis=0, concat_axis=1, tiled=True)
    moved = regroup(moved, frame_count, tile_rows, extent)
    return transform_scrambled(moved[0], moved[1], -1.0)


def to_image(spec_real, spec_imag):
    frame_count, tile_rows, extent = spec_real.shape
    row_real, row_imag = transform_last(spec_real, spec_imag, 1.0)
    packed = jnp.transpose(jnp.stack([row_real, row_imag]), (3, 0, 1, 2)).reshape(
        extent, 2 * frame_count * tile_rows
    )
    moved = lax.all_to_all(packed, "tile", split_axis=0, concat_axis=1, tiled=True)
    moved = regroup(moved, frame_count, tile_rows, extent)
    image_parts = transform_last(moved[0], moved[1], 1.0)
    return image_parts[0] / float(extent * extent)


ALL_AXES = ("grp", "tile")


def flat_index():
    return lax.axis_index("tile") * lax.axis_size("grp") + lax.axis_index("grp")


def flat_count():
    return lax.axis_size("tile") * lax.axis_size("grp")


def flat_shift(value, steps):
    tiles, groups = lax.axis_size("tile"), lax.axis_size("grp")
    count = tiles * groups
    leading, last = (max(0, -steps), min(count, count - steps))

    def place(owner):
        return (owner % groups) * tiles + owner // groups

    pairs = [(place(source), place(source + steps)) for source in range(leading, last)]
    return lax.ppermute(value, ALL_AXES, pairs)


def inverse_to_rows(spec_real, spec_imag):
    frame_count, block, extent = spec_real.shape
    tiles, groups = lax.axis_size("tile"), lax.axis_size("grp")
    owners = tiles * groups
    own_rows = extent // owners
    row_real, row_imag = transform_unscramble(spec_real, spec_imag, 1.0)
    packed = jnp.stack([row_real, row_imag]).reshape(2, frame_count, block, tiles, groups, own_rows)
    packed = jnp.transpose(packed, (4, 3, 0, 1, 2, 5)).reshape(owners, 2, frame_count, block, own_rows)
    moved = lax.all_to_all(packed, ALL_AXES, 0, 0, tiled=True)
    moved = moved.reshape(groups, tiles, 2, frame_count, block, own_rows)
    summed = jnp.sum(moved, axis=(0, 3))
    summed = jnp.transpose(summed, (1, 3, 0, 2)).reshape(2, own_rows, tiles * block)
    image_parts = transform_last(summed[0], summed[1], 1.0)
    return image_parts[0] / float(extent * extent)


def forward_from_rows(rows):
    own_rows, extent = rows.shape
    tiles, groups = lax.axis_size("tile"), lax.axis_size("grp")
    block = extent // tiles
    col_real, col_imag = transform_last(rows, None, -1.0)
    packed = jnp.stack([col_real, col_imag]).reshape(2, own_rows, tiles, block)
    packed = jnp.transpose(packed, (2, 0, 3, 1))[None]
    packed = jnp.broadcast_to(packed, (groups, tiles, 2, block, own_rows))
    packed = packed.reshape(groups * tiles, 2, block, own_rows)
    moved = lax.all_to_all(packed, ALL_AXES, 0, 0, tiled=True)
    moved = moved.reshape(groups, tiles, 2, block, own_rows)
    moved = jnp.transpose(moved, (2, 3, 1, 0, 4)).reshape(2, block, extent)
    spec_real, spec_imag = transform_scrambled(moved[0], moved[1], -1.0)
    return spec_real[None], spec_imag[None]


def denoise_rows(average):
    own_rows, extent = average.shape
    halo = 8
    total_rows = own_rows * flat_count()
    above = flat_shift(average[-halo:], 1)
    below = flat_shift(average[:halo], -1)
    padded = jnp.concatenate([above, average, below], 0)
    padded_rows = own_rows + 2 * halo
    row_index = jnp.arange(padded_rows, dtype=jnp.int32)[:, None]
    global_row = flat_index() * own_rows - halo + row_index
    col_index = jnp.arange(extent, dtype=jnp.int32)[None, :]
    keep_rows = jnp.where((global_row >= 0) & (global_row < total_rows - 1), 1.0, 0.0).astype(jnp.float32)
    keep_cols = jnp.where(col_index == extent - 1, 0.0, 1.0).astype(jnp.float32)
    zero_col = jnp.zeros((padded_rows, 1), jnp.float32)
    zero_row = jnp.zeros((1, extent), jnp.float32)

    def divergence(downward, sideways):
        prev_rows = jnp.concatenate([zero_row, downward[:-1]], 0)
        prev_cols = jnp.concatenate([zero_col, sideways[:, :-1]], 1)
        return downward - prev_rows + sideways - prev_cols

    downward = jnp.zeros_like(padded)
    sideways = jnp.zeros_like(padded)
    for sweep_index in range(TV_ITERS):
        target = divergence(downward, sideways) - padded / smooth_weight
        next_rows = jnp.concatenate([target[1:], zero_row], 0)
        grad_down = (next_rows - target) * keep_rows
        grad_side = (jnp.concatenate([target[:, 1:], zero_col], 1) - target) * keep_cols
        scaling = 1.0 + dual_step * jnp.sqrt(grad_down * grad_down + grad_side * grad_side)
        downward = (downward + dual_step * grad_down) / scaling
        sideways = (sideways + dual_step * grad_side) / scaling
    result = padded - smooth_weight * divergence(downward, sideways)
    return result[halo : halo + own_rows]


def body(frames, otf, start_image):
    frame_count = frames.shape[0]
    total_frames = float(frame_count * lax.axis_size("grp"))
    response_real = scramble_last(otf[:, 0])
    response_imag = scramble_last(otf[:, 1])
    gain = 1.0 / (response_real * response_real + response_imag * response_imag + penalty)
    both_real, both_imag = to_spectrum(jnp.concatenate([frames, start_image[None]], 0))
    data_real, data_imag = both_real[:frame_count], both_imag[:frame_count]
    weighted_real = response_real * data_real + response_imag * data_imag
    weighted_imag = response_real * data_imag - response_imag * data_real
    center_real, center_imag = both_real[frame_count:], both_imag[frame_count:]
    dual_real = jnp.zeros_like(data_real)
    dual_imag = jnp.zeros_like(data_imag)
    for iteration in range(ITERS):
        estimate_real = (weighted_real + penalty * (center_real - dual_real)) * gain
        estimate_imag = (weighted_imag + penalty * (center_imag - dual_imag)) * gain
        average = inverse_to_rows(estimate_real + dual_real, estimate_imag + dual_imag) / total_frames
        consensus_rows = denoise_rows(average)
        if iteration + 1 < ITERS:
            center_real, center_imag = forward_from_rows(consensus_rows)
            dual_real = dual_real + estimate_real - center_real
            dual_imag = dual_imag + estimate_imag - center_imag
    return lax.all_gather(consensus_rows, "grp", axis=0, tiled=True)


def solution(mesh):
    placed = (P("grp", "tile", None), P("grp", None, "tile", None), P("tile", None))
    return jax.shard_map(
        body, mesh=mesh, in_specs=placed, out_specs=P("tile", None), check_vma=False
    )
```

```python
import math

import jax
import jax.numpy as jnp
from jax import lax
from jax.sharding import PartitionSpec as P

ITERS = 2
TV_ITERS = 4


penalty = 1.0
smooth_weight = 0.25
dual_step = 0.125
highest = lax.Precision.HIGHEST


def from_behind(value, axis, steps):
    count = lax.axis_size(axis)
    leading, last = (max(0, -steps), min(count, count - steps))
    return lax.ppermute(value, axis, [(source, source + steps) for source in range(leading, last)])


def angle_table(first_count, second_count, modulus):
    left_index = jnp.arange(first_count, dtype=jnp.int32)[:, None]
    right_index = jnp.arange(second_count, dtype=jnp.int32)[None, :]
    return (left_index * right_index % modulus).astype(jnp.float32) * (2.0 * math.pi / modulus)


def mix(spec, real_part, imag_part, table_cos, table_sin, axis):
    size = table_cos.shape[1]
    table = jnp.concatenate([table_cos, table_sin], axis=1)
    if imag_part is None:
        both = jnp.einsum(spec, real_part, table, precision=highest)
        return lax.slice_in_dim(both, 0, size, axis=axis), lax.slice_in_dim(both, size, 2 * size, axis=axis)
    inputs, result = spec.split("->")
    data_spec, table_spec = inputs.split(",")
    block_spec = "c" + data_spec + ",c" + table_spec[0] + "o" + table_spec[1] + "->o" + result
    block_table = jnp.stack(
        [jnp.stack([table_cos, table_sin], 1), jnp.stack([-table_sin, table_cos], 1)]
    )
    both = jnp.einsum(block_spec, jnp.stack([real_part, imag_part]), block_table, precision=highest)
    return both[0], both[1]


def transform_last(real_part, imag_part, sign_value):
    extent = real_part.shape[-1]
    inner_size = 16
    outer_size = extent // inner_size
    leading = real_part.shape[:-1]
    first_angle = angle_table(inner_size, inner_size, inner_size)
    first_cos = jnp.cos(first_angle)
    first_sin = sign_value * jnp.sin(first_angle)
    split_real = real_part.reshape(leading + (inner_size, outer_size))
    split_imag = None if imag_part is None else imag_part.reshape(leading + (inner_size, outer_size))
    mixed_real, mixed_imag = mix("...an,ak->...kn", split_real, split_imag, first_cos, first_sin, -2)
    twist_angle = angle_table(inner_size, outer_size, extent)
    twist_cos = jnp.cos(twist_angle)
    twist_sin = sign_value * jnp.sin(twist_angle)
    turned_real = mixed_real * twist_cos - mixed_imag * twist_sin
    turned_imag = mixed_real * twist_sin + mixed_imag * twist_cos
    second_angle = angle_table(outer_size, outer_size, outer_size)
    second_cos = jnp.cos(second_angle)
    second_sin = sign_value * jnp.sin(second_angle)
    out_real, out_imag = mix("...kn,nj->...jk", turned_real, turned_imag, second_cos, second_sin, -2)
    return (out_real.reshape(leading + (extent,)), out_imag.reshape(leading + (extent,)))


def transform_scrambled(real_part, imag_part, sign_value):
    extent = real_part.shape[-1]
    inner_size = 16
    outer_size = extent // inner_size
    leading = real_part.shape[:-1]
    first_angle = angle_table(inner_size, inner_size, inner_size)
    first_cos = jnp.cos(first_angle)
    first_sin = sign_value * jnp.sin(first_angle)
    split_real = real_part.reshape(leading + (inner_size, outer_size))
    split_imag = imag_part.reshape(leading + (inner_size, outer_size))
    mixed_real, mixed_imag = mix("...an,ak->...kn", split_real, split_imag, first_cos, first_sin, -2)
    twist_angle = angle_table(inner_size, outer_size, extent)
    twist_cos = jnp.cos(twist_angle)
    twist_sin = sign_value * jnp.sin(twist_angle)
    turned_real = mixed_real * twist_cos - mixed_imag * twist_sin
    turned_imag = mixed_real * twist_sin + mixed_imag * twist_cos
    second_angle = angle_table(outer_size, outer_size, outer_size)
    second_cos = jnp.cos(second_angle)
    second_sin = sign_value * jnp.sin(second_angle)
    out_real, out_imag = mix("...kn,nj->...kj", turned_real, turned_imag, second_cos, second_sin, -1)
    return (out_real.reshape(leading + (extent,)), out_imag.reshape(leading + (extent,)))


def transform_unscramble(real_part, imag_part, sign_value):
    extent = real_part.shape[-1]
    inner_size = 16
    outer_size = extent // inner_size
    leading = real_part.shape[:-1]
    split_real = real_part.reshape(leading + (inner_size, outer_size))
    split_imag = imag_part.reshape(leading + (inner_size, outer_size))
    second_angle = angle_table(outer_size, outer_size, outer_size)
    second_cos = jnp.cos(second_angle)
    second_sin = sign_value * jnp.sin(second_angle)
    mixed_real, mixed_imag = mix("...kj,jn->...kn", split_real, split_imag, second_cos, second_sin, -1)
    twist_angle = angle_table(inner_size, outer_size, extent)
    twist_cos = jnp.cos(twist_angle)
    twist_sin = sign_value * jnp.sin(twist_angle)
    turned_real = mixed_real * twist_cos - mixed_imag * twist_sin
    turned_imag = mixed_real * twist_sin + mixed_imag * twist_cos
    first_angle = angle_table(inner_size, inner_size, inner_size)
    first_cos = jnp.cos(first_angle)
    first_sin = sign_value * jnp.sin(first_angle)
    out_real, out_imag = mix("...kn,ka->...an", turned_real, turned_imag, first_cos, first_sin, -2)
    return (out_real.reshape(leading + (extent,)), out_imag.reshape(leading + (extent,)))


def scramble_last(values):
    extent = values.shape[-1]
    inner_size = 16
    split = values.reshape(values.shape[:-1] + (extent // inner_size, inner_size))
    return jnp.swapaxes(split, -1, -2).reshape(values.shape)


def gather_groups(rows):
    groups = lax.axis_size("grp")
    position = lax.axis_index("grp")
    step = 1
    while step < groups:
        other = lax.ppermute(rows, "grp", [(source, source ^ step) for source in range(groups)])
        upper = (position // step) % 2 == 1
        rows = jnp.where(upper, jnp.concatenate([other, rows], 0), jnp.concatenate([rows, other], 0))
        step *= 2
    return rows


def regroup(moved, frame_count, tile_rows, extent):
    tiles = extent // tile_rows
    moved = moved.reshape(tile_rows, tiles, 2, frame_count, tile_rows)
    return jnp.transpose(moved, (2, 3, 0, 1, 4)).reshape(2, frame_count, tile_rows, extent)


def to_spectrum(images):
    frame_count, tile_rows, extent = images.shape
    col_real, col_imag = transform_last(images, None, -1.0)
    packed = jnp.transpose(jnp.stack([col_real, col_imag]), (3, 0, 1, 2)).reshape(
        extent, 2 * frame_count * tile_rows
    )
    moved = lax.all_to_all(packed, "tile", split_axis=0, concat_axis=1, tiled=True)
    moved = regroup(moved, frame_count, tile_rows, extent)
    return transform_scrambled(moved[0], moved[1], -1.0)


def to_image(spec_real, spec_imag):
    frame_count, tile_rows, extent = spec_real.shape
    row_real, row_imag = transform_last(spec_real, spec_imag, 1.0)
    packed = jnp.transpose(jnp.stack([row_real, row_imag]), (3, 0, 1, 2)).reshape(
        extent, 2 * frame_count * tile_rows
    )
    moved = lax.all_to_all(packed, "tile", split_axis=0, concat_axis=1, tiled=True)
    moved = regroup(moved, frame_count, tile_rows, extent)
    image_parts = transform_last(moved[0], moved[1], 1.0)
    return image_parts[0] / float(extent * extent)


ALL_AXES = ("grp", "tile")


def flat_index():
    return lax.axis_index("tile") * lax.axis_size("grp") + lax.axis_index("grp")


def flat_count():
    return lax.axis_size("tile") * lax.axis_size("grp")


def flat_shift(value, steps):
    tiles, groups = lax.axis_size("tile"), lax.axis_size("grp")
    count = tiles * groups
    leading, last = (max(0, -steps), min(count, count - steps))

    def place(owner):
        return (owner % groups) * tiles + owner // groups

    pairs = [(place(source), place(source + steps)) for source in range(leading, last)]
    return lax.ppermute(value, ALL_AXES, pairs)


def inverse_to_rows(spec_real, spec_imag):
    frame_count, block, extent = spec_real.shape
    tiles, groups = lax.axis_size("tile"), lax.axis_size("grp")
    owners = tiles * groups
    own_rows = extent // owners
    row_real, row_imag = transform_unscramble(spec_real, spec_imag, 1.0)
    packed = jnp.stack([row_real, row_imag]).reshape(2, frame_count, block, tiles, groups, own_rows)
    packed = jnp.transpose(packed, (4, 3, 0, 1, 2, 5)).reshape(owners, 2, frame_count, block, own_rows)
    moved = lax.all_to_all(packed, ALL_AXES, 0, 0, tiled=True)
    moved = moved.reshape(groups, tiles, 2, frame_count, block, own_rows)
    summed = jnp.sum(moved, axis=(0, 3))
    summed = jnp.transpose(summed, (1, 3, 0, 2)).reshape(2, own_rows, tiles * block)
    image_parts = transform_last(summed[0], summed[1], 1.0)
    return image_parts[0] / float(extent * extent)


def forward_from_rows(rows):
    own_rows, extent = rows.shape
    tiles, groups = lax.axis_size("tile"), lax.axis_size("grp")
    block = extent // tiles
    col_real, col_imag = transform_last(rows, None, -1.0)
    packed = jnp.stack([col_real, col_imag]).reshape(2, own_rows, tiles, block)
    packed = jnp.transpose(packed, (2, 0, 3, 1))[None]
    packed = jnp.broadcast_to(packed, (groups, tiles, 2, block, own_rows))
    packed = packed.reshape(groups * tiles, 2, block, own_rows)
    moved = lax.all_to_all(packed, ALL_AXES, 0, 0, tiled=True)
    moved = moved.reshape(groups, tiles, 2, block, own_rows)
    moved = jnp.transpose(moved, (2, 3, 1, 0, 4)).reshape(2, block, extent)
    spec_real, spec_imag = transform_scrambled(moved[0], moved[1], -1.0)
    return spec_real[None], spec_imag[None]


def denoise_rows(average):
    own_rows, extent = average.shape
    halo = 8
    total_rows = own_rows * flat_count()
    above = flat_shift(average[-halo:], 1)
    below = flat_shift(average[:halo], -1)
    padded = jnp.concatenate([above, average, below], 0)
    padded_rows = own_rows + 2 * halo
    row_index = jnp.arange(padded_rows, dtype=jnp.int32)[:, None]
    global_row = flat_index() * own_rows - halo + row_index
    col_index = jnp.arange(extent, dtype=jnp.int32)[None, :]
    keep_rows = jnp.where((global_row >= 0) & (global_row < total_rows - 1), 1.0, 0.0).astype(jnp.float32)
    keep_cols = jnp.where(col_index == extent - 1, 0.0, 1.0).astype(jnp.float32)
    zero_col = jnp.zeros((padded_rows, 1), jnp.float32)
    zero_row = jnp.zeros((1, extent), jnp.float32)

    def divergence(downward, sideways):
        prev_rows = jnp.concatenate([zero_row, downward[:-1]], 0)
        prev_cols = jnp.concatenate([zero_col, sideways[:, :-1]], 1)
        return downward - prev_rows + sideways - prev_cols

    downward = jnp.zeros_like(padded)
    sideways = jnp.zeros_like(padded)
    for sweep_index in range(TV_ITERS):
        target = divergence(downward, sideways) - padded / smooth_weight
        next_rows = jnp.concatenate([target[1:], zero_row], 0)
        grad_down = (next_rows - target) * keep_rows
        grad_side = (jnp.concatenate([target[:, 1:], zero_col], 1) - target) * keep_cols
        scaling = 1.0 + dual_step * jnp.sqrt(grad_down * grad_down + grad_side * grad_side)
        downward = (downward + dual_step * grad_down) / scaling
        sideways = (sideways + dual_step * grad_side) / scaling
    result = padded - smooth_weight * divergence(downward, sideways)
    return result[halo : halo + own_rows]


def body(frames, otf, start_image):
    frame_count = frames.shape[0]
    total_frames = float(frame_count * lax.axis_size("grp"))
    response_real = scramble_last(otf[:, 0])
    response_imag = scramble_last(otf[:, 1])
    gain = 1.0 / (response_real * response_real + response_imag * response_imag + penalty)
    both_real, both_imag = to_spectrum(jnp.concatenate([frames, start_image[None]], 0))
    data_real, data_imag = both_real[:frame_count], both_imag[:frame_count]
    weighted_real = response_real * data_real + response_imag * data_imag
    weighted_imag = response_real * data_imag - response_imag * data_real
    center_real, center_imag = both_real[frame_count:], both_imag[frame_count:]
    dual_real = jnp.zeros_like(data_real)
    dual_imag = jnp.zeros_like(data_imag)
    for iteration in range(ITERS):
        estimate_real = (weighted_real + penalty * (center_real - dual_real)) * gain
        estimate_imag = (weighted_imag + penalty * (center_imag - dual_imag)) * gain
        average = inverse_to_rows(estimate_real + dual_real, estimate_imag + dual_imag) / total_frames
        consensus_rows = denoise_rows(average)
        if iteration + 1 < ITERS:
            center_real, center_imag = forward_from_rows(consensus_rows)
            dual_real = dual_real + estimate_real - center_real
            dual_imag = dual_imag + estimate_imag - center_imag
    return lax.all_gather(consensus_rows, "grp", axis=0, tiled=True)


def solution(mesh):
    placed = (P("grp", "tile", None), P("grp", None, "tile", None), P("tile", None))
    return jax.shard_map(
        body, mesh=mesh, in_specs=placed, out_specs=P("tile", None), check_vma=False
    )
```

```python
import math

import jax
import jax.numpy as jnp
from jax import lax
from jax.sharding import PartitionSpec as P

ITERS = 2
TV_ITERS = 4


penalty = 1.0
smooth_weight = 0.25
dual_step = 0.125
highest = lax.Precision.HIGHEST


def from_behind(value, axis, steps):
    count = lax.axis_size(axis)
    leading, last = (max(0, -steps), min(count, count - steps))
    return lax.ppermute(value, axis, [(source, source + steps) for source in range(leading, last)])


def angle_table(first_count, second_count, modulus):
    left_index = jnp.arange(first_count, dtype=jnp.int32)[:, None]
    right_index = jnp.arange(second_count, dtype=jnp.int32)[None, :]
    return (left_index * right_index % modulus).astype(jnp.float32) * (2.0 * math.pi / modulus)


def mix(spec, real_part, imag_part, table_cos, table_sin, axis, real_only=False):
    size = table_cos.shape[1]
    table = jnp.concatenate([table_cos, table_sin], axis=1)
    if imag_part is None:
        both = jnp.einsum(spec, real_part, table, precision=highest)
        return lax.slice_in_dim(both, 0, size, axis=axis), lax.slice_in_dim(both, size, 2 * size, axis=axis)
    inputs, result = spec.split("->")
    data_spec, table_spec = inputs.split(",")
    block_spec = "c" + data_spec + ",c" + table_spec[0] + "o" + table_spec[1] + "->o" + result
    block_table = jnp.stack(
        [jnp.stack([table_cos, table_sin], 1), jnp.stack([-table_sin, table_cos], 1)]
    )
    if real_only:
        block_table = block_table[:, :, :1]
    both = jnp.einsum(block_spec, jnp.stack([real_part, imag_part]), block_table, precision=highest)
    if real_only:
        return both[0], None
    return both[0], both[1]


def transform_last(real_part, imag_part, sign_value, real_only=False):
    extent = real_part.shape[-1]
    inner_size = 16
    outer_size = extent // inner_size
    leading = real_part.shape[:-1]
    first_angle = angle_table(inner_size, inner_size, inner_size)
    first_cos = jnp.cos(first_angle)
    first_sin = sign_value * jnp.sin(first_angle)
    split_real = real_part.reshape(leading + (inner_size, outer_size))
    split_imag = None if imag_part is None else imag_part.reshape(leading + (inner_size, outer_size))
    mixed_real, mixed_imag = mix("...an,ak->...kn", split_real, split_imag, first_cos, first_sin, -2)
    twist_angle = angle_table(inner_size, outer_size, extent)
    twist_cos = jnp.cos(twist_angle)
    twist_sin = sign_value * jnp.sin(twist_angle)
    turned_real = mixed_real * twist_cos - mixed_imag * twist_sin
    turned_imag = mixed_real * twist_sin + mixed_imag * twist_cos
    second_angle = angle_table(outer_size, outer_size, outer_size)
    second_cos = jnp.cos(second_angle)
    second_sin = sign_value * jnp.sin(second_angle)
    out_real, out_imag = mix("...kn,nj->...jk", turned_real, turned_imag, second_cos, second_sin, -2, real_only)
    if real_only:
        return out_real.reshape(leading + (extent,)), None
    return (out_real.reshape(leading + (extent,)), out_imag.reshape(leading + (extent,)))


def transform_scrambled(real_part, imag_part, sign_value):
    extent = real_part.shape[-1]
    inner_size = 16
    outer_size = extent // inner_size
    leading = real_part.shape[:-1]
    first_angle = angle_table(inner_size, inner_size, inner_size)
    first_cos = jnp.cos(first_angle)
    first_sin = sign_value * jnp.sin(first_angle)
    split_real = real_part.reshape(leading + (inner_size, outer_size))
    split_imag = imag_part.reshape(leading + (inner_size, outer_size))
    mixed_real, mixed_imag = mix("...an,ak->...kn", split_real, split_imag, first_cos, first_sin, -2)
    twist_angle = angle_table(inner_size, outer_size, extent)
    twist_cos = jnp.cos(twist_angle)
    twist_sin = sign_value * jnp.sin(twist_angle)
    turned_real = mixed_real * twist_cos - mixed_imag * twist_sin
    turned_imag = mixed_real * twist_sin + mixed_imag * twist_cos
    second_angle = angle_table(outer_size, outer_size, outer_size)
    second_cos = jnp.cos(second_angle)
    second_sin = sign_value * jnp.sin(second_angle)
    out_real, out_imag = mix("...kn,nj->...kj", turned_real, turned_imag, second_cos, second_sin, -1)
    return (out_real.reshape(leading + (extent,)), out_imag.reshape(leading + (extent,)))


def transform_unscramble(real_part, imag_part, sign_value):
    extent = real_part.shape[-1]
    inner_size = 16
    outer_size = extent // inner_size
    leading = real_part.shape[:-1]
    split_real = real_part.reshape(leading + (inner_size, outer_size))
    split_imag = imag_part.reshape(leading + (inner_size, outer_size))
    second_angle = angle_table(outer_size, outer_size, outer_size)
    second_cos = jnp.cos(second_angle)
    second_sin = sign_value * jnp.sin(second_angle)
    mixed_real, mixed_imag = mix("...kj,jn->...kn", split_real, split_imag, second_cos, second_sin, -1)
    twist_angle = angle_table(inner_size, outer_size, extent)
    twist_cos = jnp.cos(twist_angle)
    twist_sin = sign_value * jnp.sin(twist_angle)
    turned_real = mixed_real * twist_cos - mixed_imag * twist_sin
    turned_imag = mixed_real * twist_sin + mixed_imag * twist_cos
    first_angle = angle_table(inner_size, inner_size, inner_size)
    first_cos = jnp.cos(first_angle)
    first_sin = sign_value * jnp.sin(first_angle)
    out_real, out_imag = mix("...kn,ka->...an", turned_real, turned_imag, first_cos, first_sin, -2)
    return (out_real.reshape(leading + (extent,)), out_imag.reshape(leading + (extent,)))


def scramble_last(values):
    extent = values.shape[-1]
    inner_size = 16
    split = values.reshape(values.shape[:-1] + (extent // inner_size, inner_size))
    return jnp.swapaxes(split, -1, -2).reshape(values.shape)


def gather_groups(rows):
    groups = lax.axis_size("grp")
    position = lax.axis_index("grp")
    step = 1
    while step < groups:
        other = lax.ppermute(rows, "grp", [(source, source ^ step) for source in range(groups)])
        upper = (position // step) % 2 == 1
        rows = jnp.where(upper, jnp.concatenate([other, rows], 0), jnp.concatenate([rows, other], 0))
        step *= 2
    return rows


def regroup(moved, frame_count, tile_rows, extent):
    tiles = extent // tile_rows
    moved = moved.reshape(tile_rows, tiles, 2, frame_count, tile_rows)
    return jnp.transpose(moved, (2, 3, 0, 1, 4)).reshape(2, frame_count, tile_rows, extent)


def to_spectrum(images):
    frame_count, tile_rows, extent = images.shape
    col_real, col_imag = transform_last(images, None, -1.0)
    packed = jnp.transpose(jnp.stack([col_real, col_imag]), (3, 0, 1, 2)).reshape(
        extent, 2 * frame_count * tile_rows
    )
    moved = lax.all_to_all(packed, "tile", split_axis=0, concat_axis=1, tiled=True)
    moved = regroup(moved, frame_count, tile_rows, extent)
    return transform_scrambled(moved[0], moved[1], -1.0)


def to_image(spec_real, spec_imag):
    frame_count, tile_rows, extent = spec_real.shape
    row_real, row_imag = transform_last(spec_real, spec_imag, 1.0)
    packed = jnp.transpose(jnp.stack([row_real, row_imag]), (3, 0, 1, 2)).reshape(
        extent, 2 * frame_count * tile_rows
    )
    moved = lax.all_to_all(packed, "tile", split_axis=0, concat_axis=1, tiled=True)
    moved = regroup(moved, frame_count, tile_rows, extent)
    image_parts = transform_last(moved[0], moved[1], 1.0)
    return image_parts[0] / float(extent * extent)


ALL_AXES = ("grp", "tile")


def flat_index():
    return lax.axis_index("tile") * lax.axis_size("grp") + lax.axis_index("grp")


def flat_count():
    return lax.axis_size("tile") * lax.axis_size("grp")


def flat_shift(value, steps):
    tiles, groups = lax.axis_size("tile"), lax.axis_size("grp")
    count = tiles * groups
    leading, last = (max(0, -steps), min(count, count - steps))

    def place(owner):
        return (owner % groups) * tiles + owner // groups

    pairs = [(place(source), place(source + steps)) for source in range(leading, last)]
    return lax.ppermute(value, ALL_AXES, pairs)


def inverse_to_rows(spec_real, spec_imag):
    frame_count, block, extent = spec_real.shape
    tiles, groups = lax.axis_size("tile"), lax.axis_size("grp")
    owners = tiles * groups
    own_rows = extent // owners
    row_real, row_imag = transform_unscramble(spec_real, spec_imag, 1.0)
    packed = jnp.stack([row_real, row_imag]).reshape(2, frame_count, block, tiles, groups, own_rows)
    packed = jnp.transpose(packed, (4, 3, 0, 1, 2, 5)).reshape(owners, 2, frame_count, block, own_rows)
    moved = lax.all_to_all(packed, ALL_AXES, 0, 0, tiled=True)
    moved = moved.reshape(groups, tiles, 2, frame_count, block, own_rows)
    summed = jnp.sum(moved, axis=(0, 3))
    summed = jnp.transpose(summed, (1, 3, 0, 2)).reshape(2, own_rows, tiles * block)
    image_parts = transform_last(summed[0], summed[1], 1.0, real_only=True)
    return image_parts[0] / float(extent * extent)


def forward_from_rows(rows):
    own_rows, extent = rows.shape
    tiles, groups = lax.axis_size("tile"), lax.axis_size("grp")
    block = extent // tiles
    col_real, col_imag = transform_last(rows, None, -1.0)
    packed = jnp.stack([col_real, col_imag]).reshape(2, own_rows, tiles, block)
    packed = jnp.transpose(packed, (2, 0, 3, 1))[None]
    packed = jnp.broadcast_to(packed, (groups, tiles, 2, block, own_rows))
    packed = packed.reshape(groups * tiles, 2, block, own_rows)
    moved = lax.all_to_all(packed, ALL_AXES, 0, 0, tiled=True)
    moved = moved.reshape(groups, tiles, 2, block, own_rows)
    moved = jnp.transpose(moved, (2, 3, 1, 0, 4)).reshape(2, block, extent)
    spec_real, spec_imag = transform_scrambled(moved[0], moved[1], -1.0)
    return spec_real[None], spec_imag[None]


def denoise_rows(average):
    own_rows, extent = average.shape
    halo = 8
    total_rows = own_rows * flat_count()
    above = flat_shift(average[-halo:], 1)
    below = flat_shift(average[:halo], -1)
    padded = jnp.concatenate([above, average, below], 0)
    padded_rows = own_rows + 2 * halo
    row_index = jnp.arange(padded_rows, dtype=jnp.int32)[:, None]
    global_row = flat_index() * own_rows - halo + row_index
    col_index = jnp.arange(extent, dtype=jnp.int32)[None, :]
    keep_rows = jnp.where((global_row >= 0) & (global_row < total_rows - 1), 1.0, 0.0).astype(jnp.float32)
    keep_cols = jnp.where(col_index == extent - 1, 0.0, 1.0).astype(jnp.float32)
    zero_col = jnp.zeros((padded_rows, 1), jnp.float32)
    zero_row = jnp.zeros((1, extent), jnp.float32)

    def divergence(downward, sideways):
        prev_rows = jnp.concatenate([zero_row, downward[:-1]], 0)
        prev_cols = jnp.concatenate([zero_col, sideways[:, :-1]], 1)
        return downward - prev_rows + sideways - prev_cols

    downward = jnp.zeros_like(padded)
    sideways = jnp.zeros_like(padded)
    for sweep_index in range(TV_ITERS):
        target = divergence(downward, sideways) - padded / smooth_weight
        next_rows = jnp.concatenate([target[1:], zero_row], 0)
        grad_down = (next_rows - target) * keep_rows
        grad_side = (jnp.concatenate([target[:, 1:], zero_col], 1) - target) * keep_cols
        scaling = 1.0 + dual_step * jnp.sqrt(grad_down * grad_down + grad_side * grad_side)
        downward = (downward + dual_step * grad_down) / scaling
        sideways = (sideways + dual_step * grad_side) / scaling
    result = padded - smooth_weight * divergence(downward, sideways)
    return result[halo : halo + own_rows]


def body(frames, otf, start_image):
    frame_count = frames.shape[0]
    total_frames = float(frame_count * lax.axis_size("grp"))
    response_real = scramble_last(otf[:, 0])
    response_imag = scramble_last(otf[:, 1])
    gain = 1.0 / (response_real * response_real + response_imag * response_imag + penalty)
    both_real, both_imag = to_spectrum(jnp.concatenate([frames, start_image[None]], 0))
    data_real, data_imag = both_real[:frame_count], both_imag[:frame_count]
    weighted_real = response_real * data_real + response_imag * data_imag
    weighted_imag = response_real * data_imag - response_imag * data_real
    center_real, center_imag = both_real[frame_count:], both_imag[frame_count:]
    dual_real = jnp.zeros_like(data_real)
    dual_imag = jnp.zeros_like(data_imag)
    for iteration in range(ITERS):
        estimate_real = (weighted_real + penalty * (center_real - dual_real)) * gain
        estimate_imag = (weighted_imag + penalty * (center_imag - dual_imag)) * gain
        average = inverse_to_rows(estimate_real + dual_real, estimate_imag + dual_imag) / total_frames
        consensus_rows = denoise_rows(average)
        if iteration + 1 < ITERS:
            center_real, center_imag = forward_from_rows(consensus_rows)
            dual_real = dual_real + estimate_real - center_real
            dual_imag = dual_imag + estimate_imag - center_imag
    return lax.all_gather(consensus_rows, "grp", axis=0, tiled=True)


def solution(mesh):
    placed = (P("grp", "tile", None), P("grp", None, "tile", None), P("tile", None))
    return jax.shard_map(
        body, mesh=mesh, in_specs=placed, out_specs=P("tile", None), check_vma=False
    )
```
